32 devices in a mesh: batch: 8 (over z, y), width: 4 (over x, core).
Axes of the slice: x: 2, y: 2, z: 4, core: 2. Of those that a mesh axis runs over, the one named last changes fastest.
Arguments:
- teacher: bfloat16 [2048, 4096], P('batch', 'width'), may hold values from -48 to 48, as said below
- student: bfloat16 [2048, 1024], P('batch', 'width'), may hold values from -48 to 48, as said below
Outputs:
- grad: float32 [2048, 1024], P('batch', 'width')
The draws below stay inside these ranges and needn't reach their ends.
Inputs may be any that keep to these rules, and one draw needn't show every extreme that they name: `teacher`: Real-valued embeddings. `student`: Real-valued embeddings.
All inputs are finite; a program needn't handle non-finite values.
Results may differ from the reference program's by a relative error of at most 0.00075.
Values may be sent and summed in bfloat16 or wider, within the bound.
No kernel may reach another device: no remote copies, remote signals or barrier semaphores. Data moves between devices by JAX's collectives and lax.ppermute only.
A program may use at most 64 MiB of HBM per device.

```python
import math
import jax
import jax.numpy as jnp
from jax import lax

DT = 4096
DS = 1024
ROWS_DEV = 256
REACH = 4
ROWS = 2048
NEAR = 2304
N_BATCH = 8


def row_scales(key):
    place = jnp.arange(ROWS, dtype=jnp.float32) / max(ROWS - 1, 1)
    spread = jax.random.uniform(jax.random.fold_in(key, 5), (ROWS, 1), minval=math.log(1.2), maxval=math.log(4.8))
    return jnp.exp(spread) * (0.5 + place[:, None])


def draw_teacher(key, part):
    scales = row_scales(key)
    second = jax.random.fold_in(jax.random.fold_in(key, 11), 0)
    values = scales * jnp.clip(jax.random.normal(second, (ROWS, DT)), -6.0, 6.0)
    return values.astype(jnp.bfloat16)


def draw_student(key, part):
    scales = row_scales(key)
    second = jax.random.fold_in(jax.random.fold_in(key, 23), 0)
    values = scales * jnp.clip(jax.random.normal(second, (ROWS, DS)), -6.0, 6.0)
    return values.astype(jnp.bfloat16)


def setup_inputs(seed: int = 0) -> dict:
    splits = jax.random.split(jax.random.key(seed), 3)
    teacher = draw_teacher(jax.random.fold_in(splits[2], 71), 0)
    student = draw_student(jax.random.fold_in(splits[2], 71), 0)
    return dict(teacher=teacher, student=student)


def reference(teacher, student):
    teacher_wide = teacher.astype(jnp.float32)
    student_wide = student.astype(jnp.float32)
    teacher_sq = jnp.sum(teacher_wide * teacher_wide, axis=1) / DT
    student_sq = jnp.sum(student_wide * student_wide, axis=1) / DS
    width_band = 2 * REACH + 1
    teacher_blocks = jnp.pad(teacher_wide.reshape(N_BATCH, ROWS_DEV, DT), ((REACH, REACH), (0, 0), (0, 0)))
    student_blocks = jnp.pad(student_wide.reshape(N_BATCH, ROWS_DEV, DS), ((REACH, REACH), (0, 0), (0, 0)))
    student_lowpad = jnp.pad(student.reshape(N_BATCH, ROWS_DEV, DS), ((REACH, REACH), (0, 0), (0, 0)))
    tsq_blocks = jnp.pad(teacher_sq.reshape(N_BATCH, ROWS_DEV), ((REACH, REACH), (0, 0)))
    ssq_blocks = jnp.pad(student_sq.reshape(N_BATCH, ROWS_DEV), ((REACH, REACH), (0, 0)))
    offsets = jnp.arange(width_band, dtype=jnp.int32) - REACH

    def one(block):
        start = block.astype(jnp.int32)
        own_t = lax.dynamic_index_in_dim(teacher_blocks, start + REACH, 0, keepdims=False)
        own_s = lax.dynamic_index_in_dim(student_blocks, start + REACH, 0, keepdims=False)
        own_tsq = lax.dynamic_index_in_dim(tsq_blocks, start + REACH, 0, keepdims=False)
        own_ssq = lax.dynamic_index_in_dim(ssq_blocks, start + REACH, 0, keepdims=False)
        win_t = lax.dynamic_slice_in_dim(teacher_blocks, start, width_band, 0).reshape(NEAR, DT)
        win_s = lax.dynamic_slice_in_dim(student_blocks, start, width_band, 0).reshape(NEAR, DS)
        win_low = lax.dynamic_slice_in_dim(student_lowpad, start, width_band, 0).reshape(NEAR, DS)
        win_tsq = lax.dynamic_slice_in_dim(tsq_blocks, start, width_band, 0).reshape(NEAR)
        win_ssq = lax.dynamic_slice_in_dim(ssq_blocks, start, width_band, 0).reshape(NEAR)
        tgram = jnp.dot(own_t, win_t.T, precision=lax.Precision.HIGHEST)
        sgram = jnp.dot(own_s, win_s.T, precision=lax.Precision.HIGHEST)
        sdist = own_ssq[:, None] + win_ssq[None, :] - 2.0 * sgram / DS
        tdist = own_tsq[:, None] + win_tsq[None, :] - 2.0 * tgram / DT
        partner = start + offsets
        valid = jnp.logical_and(partner >= 0, partner < N_BATCH)
        valid_cols = jnp.repeat(valid, ROWS_DEV)
        residual = jnp.where(valid_cols[None, :], sdist - tdist, jnp.zeros_like(sdist))
        row_total = jnp.sum(residual, axis=1)
        residual_low = residual.astype(jnp.bfloat16)
        pulled = jnp.dot(residual_low, win_low, preferred_element_type=jnp.float32)
        return (own_s * row_total[:, None] - pulled) / NEAR

    grads = lax.map(one, jnp.arange(N_BATCH, dtype=jnp.int32))
    return grads.reshape(ROWS, DS)
```

```python
import jax
import jax.numpy as jnp
from jax import lax
from jax.sharding import PartitionSpec as P

REACH = 4


def shifted(block, axis, distance):
    size = lax.axis_size(axis)
    route = [(i + distance, i) for i in range(size) if 0 <= i + distance < size]
    return lax.ppermute(block, axis, route)


def body(teacher, student):
    group = lax.axis_size("batch")
    owner = lax.axis_index("batch")
    width = lax.axis_size("width")
    rows_dev = teacher.shape[0]
    dt = teacher.shape[1] * width
    ds = student.shape[1] * width
    reach = min(REACH, group - 1)
    near_count = (2 * REACH + 1) * rows_dev

    teacher_band = [teacher]
    student_band = [student]
    for d in range(1, reach + 1):
        t_d, s_d = shifted((teacher, student), "batch", d)
        teacher_band.append(t_d)
        student_band.append(s_d)

    def sq(x):
        xf = x.astype(jnp.float32)
        return jnp.sum(xf * xf, axis=1)

    gram_parts = []
    q_parts = []
    for t_d, s_d in zip(teacher_band, student_band):
        tg = lax.dot_general(teacher, t_d, (((1,), (1,)), ((), ())), preferred_element_type=jnp.float32)
        sg = lax.dot_general(student, s_d, (((1,), (1,)), ((), ())), preferred_element_type=jnp.float32)
        gram_parts.append(sg * (2.0 / ds) - tg * (2.0 / dt))
        q_parts.append(sq(s_d) / ds - sq(t_d) / dt)
    gram = lax.psum(jnp.stack(gram_parts), "width")
    q = lax.psum(jnp.stack(q_parts), "width")

    own_q = q[0]
    student_f = student.astype(jnp.float32)
    row_total = jnp.zeros((rows_dev,), jnp.float32)
    pulled = jnp.zeros(student.shape, jnp.float32)
    for d in range(reach + 1):
        resid = own_q[:, None] + q[d][None, :] - gram[d]
        if d > 0:
            valid = owner + d < group
            resid = jnp.where(valid, resid, jnp.zeros_like(resid))
        low = resid.astype(jnp.bfloat16)
        row_total = row_total + jnp.sum(resid, axis=1)
        pulled = pulled + jnp.dot(low, student_band[d], preferred_element_type=jnp.float32)
        if d > 0:
            back = lax.dot_general(low, student, (((0,), (0,)), ((), ())), preferred_element_type=jnp.float32)
            col = jnp.sum(resid, axis=0)
            back_r, col_r = shifted((back, col), "batch", -d)
            pulled = pulled + back_r
            row_total = row_total + col_r
    grad = (student_f * row_total[:, None] - pulled) / near_count
    return grad


def solution(mesh):
    in_specs = (P("batch", "width"), P("batch", "width"))
    out_specs = P("batch", "width")
    return jax.shard_map(body, mesh=mesh, in_specs=in_specs, out_specs=out_specs, check_vma=False)
```

```python
import jax
import jax.numpy as jnp
from jax import lax
from jax.sharding import PartitionSpec as P

REACH = 4


def shifted(block, axis, distance):
    size = lax.axis_size(axis)
    route = [(i + distance, i) for i in range(size) if 0 <= i + distance < size]
    return lax.ppermute(block, axis, route)


def swapped(block, axis, mask):
    size = lax.axis_size(axis)
    return lax.ppermute(block, axis, [(i, i ^ mask) for i in range(size)])


def halves(x, axis, bit):
    half = x.shape[axis] // 2
    mine = (lax.axis_index("width") // bit) % 2
    keep = lax.dynamic_slice_in_dim(x, mine * half, half, axis)
    send = lax.dynamic_slice_in_dim(x, (1 - mine) * half, half, axis)
    return keep, send, mine


def joined(keep, got, axis, mine):
    first = jnp.where(mine == 0, keep, got)
    second = jnp.where(mine == 0, got, keep)
    return jnp.concatenate([first, second], axis=axis)


def width_sum(x):
    width = lax.axis_size("width")
    if width != 4:
        return lax.psum(x, "width")
    keep, send, core = halves(x, 2, 1)
    part = keep + swapped(send, "width", 1)
    keep, send, chip = halves(part, 1, 2)
    part = keep + swapped(send, "width", 2)
    part = joined(part, swapped(part, "width", 2), 1, chip)
    return joined(part, swapped(part, "width", 1), 2, core)


def body(teacher, student):
    group = lax.axis_size("batch")
    owner = lax.axis_index("batch")
    width = lax.axis_size("width")
    rows_dev = teacher.shape[0]
    ft = teacher.shape[1]
    fs = student.shape[1]
    dt = ft * width
    ds = fs * width
    reach = min(REACH, group - 1)
    near_count = (2 * REACH + 1) * rows_dev

    both = jnp.concatenate([teacher, student], axis=1)
    teacher_band = [teacher]
    student_band = [student]
    for d in range(1, reach + 1):
        got = shifted(both, "batch", d)
        teacher_band.append(got[:, :ft])
        student_band.append(got[:, ft:])

    def sq(x):
        xf = x.astype(jnp.float32)
        return jnp.sum(xf * xf, axis=1)

    pad = (-(rows_dev + 1)) % 8
    parts = []
    for t_d, s_d in zip(teacher_band, student_band):
        tg = lax.dot_general(teacher, t_d, (((1,), (1,)), ((), ())), preferred_element_type=jnp.float32)
        sg = lax.dot_general(student, s_d, (((1,), (1,)), ((), ())), preferred_element_type=jnp.float32)
        q_d = sq(s_d) / ds - sq(t_d) / dt
        parts.append(jnp.concatenate(
            [sg * (2.0 / ds) - tg * (2.0 / dt), q_d[None, :], jnp.zeros((pad, rows_dev), jnp.float32)], axis=0))
    total = width_sum(jnp.stack(parts))
    gram = total[:, :rows_dev, :]
    q = total[:, rows_dev, :]

    own_q = q[0]
    student_f = student.astype(jnp.float32)
    row_total = jnp.zeros((rows_dev,), jnp.float32)
    pulled = jnp.zeros(student.shape, jnp.float32)
    for d in range(reach + 1):
        resid = own_q[:, None] + q[d][None, :] - gram[d]
        if d > 0:
            valid = owner + d < group
            resid = jnp.where(valid, resid, jnp.zeros_like(resid))
        low = resid.astype(jnp.bfloat16)
        row_total = row_total + jnp.sum(resid, axis=1)
        pulled = pulled + jnp.dot(low, student_band[d], preferred_element_type=jnp.float32)
        if d > 0:
            back = lax.dot_general(low, student, (((0,), (0,)), ((), ())), preferred_element_type=jnp.float32)
            col = jnp.sum(resid, axis=0)
            if fs == rows_dev:
                got = shifted(jnp.concatenate([back, col[None, :]], axis=0), "batch", -d)
                pulled = pulled + got[:rows_dev]
                row_total = row_total + got[rows_dev]
            else:
                back_r, col_r = shifted((back, col), "batch", -d)
                pulled = pulled + back_r
                row_total = row_total + col_r
    grad = (student_f * row_total[:, None] - pulled) / near_count
    return grad


def solution(mesh):
    in_specs = (P("batch", "width"), P("batch", "width"))
    out_specs = P("batch", "width")
    return jax.shard_map(body, mesh=mesh, in_specs=in_specs, out_specs=out_specs, check_vma=False)
```

```python
import jax
import jax.numpy as jnp
from jax import lax
from jax.sharding import PartitionSpec as P

REACH = 4


def shifted(block, axis, distance):
    size = lax.axis_size(axis)
    route = [(i + distance, i) for i in range(size) if 0 <= i + distance < size]
    return lax.ppermute(block, axis, route)


def swapped(block, axis, mask):
    size = lax.axis_size(axis)
    return lax.ppermute(block, axis, [(i, i ^ mask) for i in range(size)])


def halves(x, axis, bit):
    half = x.shape[axis] // 2
    mine = (lax.axis_index("width") // bit) % 2
    keep = lax.dynamic_slice_in_dim(x, mine * half, half, axis)
    send = lax.dynamic_slice_in_dim(x, (1 - mine) * half, half, axis)
    return keep, send, mine


def joined(keep, got, axis, mine):
    first = jnp.where(mine == 0, keep, got)
    second = jnp.where(mine == 0, got, keep)
    return jnp.concatenate([first, second], axis=axis)


def width_sum(x):
    width = lax.axis_size("width")
    if width != 4:
        return lax.psum(x, "width")
    keep, send, core = halves(x, 2, 1)
    part = keep + swapped(send, "width", 1)
    keep, send, chip = halves(part, 1, 2)
    part = keep + swapped(send, "width", 2)
    part = joined(part, swapped(part, "width", 2), 1, chip)
    return joined(part, swapped(part, "width", 1), 2, core)


def body(teacher, student):
    group = lax.axis_size("batch")
    owner = lax.axis_index("batch")
    width = lax.axis_size("width")
    rows_dev = teacher.shape[0]
    ft = teacher.shape[1]
    fs = student.shape[1]
    dt = ft * width
    ds = fs * width
    reach = min(REACH, group - 1)
    near_count = (2 * REACH + 1) * rows_dev

    offsets = [0] + [d if d % 2 else -d for d in range(1, reach + 1)]
    both = jnp.concatenate([teacher, student], axis=1)
    teacher_band = [teacher]
    student_band = [student]
    for e in offsets[1:]:
        got = shifted(both, "batch", e)
        teacher_band.append(got[:, :ft])
        student_band.append(got[:, ft:])

    def sq(x):
        xf = x.astype(jnp.float32)
        return jnp.sum(xf * xf, axis=1)

    pad = (-(rows_dev + 1)) % 8
    parts = []
    for t_d, s_d in zip(teacher_band, student_band):
        tg = lax.dot_general(teacher, t_d, (((1,), (1,)), ((), ())), preferred_element_type=jnp.float32)
        sg = lax.dot_general(student, s_d, (((1,), (1,)), ((), ())), preferred_element_type=jnp.float32)
        q_d = sq(s_d) / ds - sq(t_d) / dt
        parts.append(jnp.concatenate(
            [sg * (2.0 / ds) - tg * (2.0 / dt), q_d[None, :], jnp.zeros((pad, rows_dev), jnp.float32)], axis=0))
    total = width_sum(jnp.stack(parts))
    gram = total[:, :rows_dev, :]
    q = total[:, rows_dev, :]

    own_q = q[0]
    student_f = student.astype(jnp.float32)
    row_total = jnp.zeros((rows_dev,), jnp.float32)
    pulled = jnp.zeros(student.shape, jnp.float32)
    for d, e in enumerate(offsets):
        resid = own_q[:, None] + q[d][None, :] - gram[d]
        if d > 0:
            valid = jnp.logical_and(owner + e >= 0, owner + e < group)
            resid = jnp.where(valid, resid, jnp.zeros_like(resid))
        low = resid.astype(jnp.bfloat16)
        row_total = row_total + jnp.sum(resid, axis=1)
        pulled = pulled + jnp.dot(low, student_band[d], preferred_element_type=jnp.float32)
        if d > 0:
            back = lax.dot_general(low, student, (((0,), (0,)), ((), ())), preferred_element_type=jnp.float32)
            col = jnp.sum(resid, axis=0)
            if fs == rows_dev:
                got = shifted(jnp.concatenate([back, col[None, :]], axis=0), "batch", -e)
                pulled = pulled + got[:rows_dev]
                row_total = row_total + got[rows_dev]
            else:
                back_r, col_r = shifted((back, col), "batch", -e)
                pulled = pulled + back_r
                row_total = row_total + col_r
    grad = (student_f * row_total[:, None] - pulled) / near_count
    return grad


def solution(mesh):
    in_specs = (P("batch", "width"), P("batch", "width"))
    out_specs = P("batch", "width")
    return jax.shard_map(body, mesh=mesh, in_specs=in_specs, out_specs=out_specs, check_vma=False)
```

```python
import jax
import jax.numpy as jnp
from jax import lax
from jax.sharding import PartitionSpec as P

REACH = 4


def shifted(block, axis, distance):
    size = lax.axis_size(axis)
    route = [(i + distance, i) for i in range(size) if 0 <= i + distance < size]
    return lax.ppermute(block, axis, route)


def swapped(block, axis, mask):
    size = lax.axis_size(axis)
    return lax.ppermute(block, axis, [(i, i ^ mask) for i in range(size)])


def halves(x, axis, bit):
    half = x.shape[axis] // 2
    mine = (lax.axis_index("width") // bit) % 2
    keep = lax.dynamic_slice_in_dim(x, mine * half, half, axis)
    send = lax.dynamic_slice_in_dim(x, (1 - mine) * half, half, axis)
    return keep, send, mine


def joined(keep, got, axis, mine):
    first = jnp.where(mine == 0, keep, got)
    second = jnp.where(mine == 0, got, keep)
    return jnp.concatenate([first, second], axis=axis)


def width_sum(x):
    width = lax.axis_size("width")
    if width != 4:
        return lax.psum(x, "width")
    keep, send, core = halves(x, 2, 1)
    part = keep + swapped(send, "width", 1)
    keep, send, chip = halves(part, 1, 2)
    part = keep + swapped(send, "width", 2)
    part = joined(part, swapped(part, "width", 2), 1, chip)
    return joined(part, swapped(part, "width", 1), 2, core)


def body(teacher, student):
    group = lax.axis_size("batch")
    owner = lax.axis_index("batch")
    width = lax.axis_size("width")
    rows_dev = teacher.shape[0]
    ft = teacher.shape[1]
    fs = student.shape[1]
    dt = ft * width
    ds = fs * width
    reach = min(REACH, group - 1)
    near_count = (2 * REACH + 1) * rows_dev

    offsets = [0] + [d if d % 2 else -d for d in range(1, reach + 1)]
    both = jnp.concatenate([teacher, student], axis=1)
    teacher_band = [teacher]
    student_band = [student]
    for e in offsets[1:]:
        got = shifted(both, "batch", e)
        teacher_band.append(got[:, :ft])
        student_band.append(got[:, ft:])

    def sq(x):
        xf = x.astype(jnp.float32)
        return jnp.sum(xf * xf, axis=1)

    pad = (-(rows_dev + 1)) % 8

    def tile_part(t_d, s_d):
        tg = lax.dot_general(teacher, t_d, (((1,), (1,)), ((), ())), preferred_element_type=jnp.float32)
        sg = lax.dot_general(student, s_d, (((1,), (1,)), ((), ())), preferred_element_type=jnp.float32)
        q_d = sq(s_d) / ds - sq(t_d) / dt
        return jnp.concatenate(
            [sg * (2.0 / ds) - tg * (2.0 / dt), q_d[None, :], jnp.zeros((pad, rows_dev), jnp.float32)], axis=0)

    student_f = student.astype(jnp.float32)
    row_total = jnp.zeros((rows_dev,), jnp.float32)
    pulled = jnp.zeros(student.shape, jnp.float32)
    own_q = None
    split = min(3, len(offsets))
    for group_idx in ([list(range(split)), list(range(split, len(offsets)))]):
        if not group_idx:
            continue
        total = width_sum(jnp.stack([tile_part(teacher_band[d], student_band[d]) for d in group_idx]))
        if own_q is None:
            own_q = total[0, rows_dev, :]
        for k, d in enumerate(group_idx):
            e = offsets[d]
            resid = own_q[:, None] + total[k, rows_dev, :][None, :] - total[k, :rows_dev, :]
            if d > 0:
                valid = jnp.logical_and(owner + e >= 0, owner + e < group)
                resid = jnp.where(valid, resid, jnp.zeros_like(resid))
            low = resid.astype(jnp.bfloat16)
            row_total = row_total + jnp.sum(resid, axis=1)
            pulled = pulled + jnp.dot(low, student_band[d], preferred_element_type=jnp.float32)
            if d > 0:
                back = lax.dot_general(low, student, (((0,), (0,)), ((), ())), preferred_element_type=jnp.float32)
                col = jnp.sum(resid, axis=0)
                if fs == rows_dev:
                    got = shifted(jnp.concatenate([back, col[None, :]], axis=0), "batch", -e)
                    pulled = pulled + got[:rows_dev]
                    row_total = row_total + got[rows_dev]
                else:
                    back_r, col_r = shifted((back, col), "batch", -e)
                    pulled = pulled + back_r
                    row_total = row_total + col_r
    grad = (student_f * row_total[:, None] - pulled) / near_count
    return grad


def solution(mesh):
    in_specs = (P("batch", "width"), P("batch", "width"))
    out_specs = P("batch", "width")
    return jax.shard_map(body, mesh=mesh, in_specs=in_specs, out_specs=out_specs, check_vma=False)
```

```python
import jax
import jax.numpy as jnp
from jax import lax
from jax.sharding import PartitionSpec as P

REACH = 4


def shifted(block, axis, distance):
    size = lax.axis_size(axis)
    route = [(i + distance, i) for i in range(size) if 0 <= i + distance < size]
    return lax.ppermute(block, axis, route)


def swapped(block, axis, mask):
    size = lax.axis_size(axis)
    return lax.ppermute(block, axis, [(i, i ^ mask) for i in range(size)])


def split_sum(x, axis, mask, bit):
    keep = lax.dynamic_index_in_dim(x, bit, axis, keepdims=False)
    send = lax.dynamic_index_in_dim(x, 1 - bit, axis, keepdims=False)
    return keep + swapped(send, "width", mask)


def gathered(x, axis, mask, bit):
    got = swapped(x, "width", mask)
    first = jnp.where(bit == 0, x, got)
    second = jnp.where(bit == 0, got, x)
    return jnp.stack([first, second], axis=axis)


def body(teacher, student):
    group = lax.axis_size("batch")
    owner = lax.axis_index("batch")
    width = lax.axis_size("width")
    widx = lax.axis_index("width")
    core_bit = widx % 2
    chip_bit = (widx // 2) % 2
    n = teacher.shape[0]
    ft = teacher.shape[1]
    fs = student.shape[1]
    dt = ft * width
    ds = fs * width
    m = n // 4
    reach = min(REACH, group - 1)
    near_count = (2 * REACH + 1) * n

    offsets = [d if d % 2 else -d for d in range(1, reach + 1)]
    both = jnp.concatenate([teacher, student], axis=1)
    blocks = [shifted(both, "batch", e) for e in offsets]
    givers = [shifted(student, "batch", -e) for e in offsets]
    t_band = [teacher] + [b[:, :ft] for b in blocks]
    s_band = [student] + [b[:, ft:] for b in blocks]
    tiles = len(t_band)

    def sq(x):
        xf = x.astype(jnp.float32)
        return jnp.sum(xf * xf, axis=1)

    own_q = sq(student) / ds - sq(teacher) / dt
    zero = jnp.zeros((n,), jnp.float32)
    parts = []
    for k in range(tiles):
        tg = lax.dot_general(teacher, t_band[k], (((1,), (1,)), ((), ())), preferred_element_type=jnp.float32)
        sg = lax.dot_general(student, s_band[k], (((1,), (1,)), ((), ())), preferred_element_type=jnp.float32)
        g = sg * (2.0 / ds) - tg * (2.0 / dt)
        q_p = own_q if k == 0 else sq(s_band[k]) / ds - sq(t_band[k]) / dt
        extra = jnp.stack([q_p, own_q if k == 0 else zero, jnp.sum(g, axis=0), jnp.sum(g, axis=1)]
                          + [zero] * 4)
        chunks = jnp.concatenate([g.reshape(4, m, n), jnp.broadcast_to(extra, (4, 8, n))], axis=1)
        parts.append(chunks.reshape(2, 2, m + 8, n))
    mine = split_sum(jnp.stack(parts), 2, 1, core_bit)
    mine = split_sum(mine, 1, 2, chip_bit)

    q_p = mine[:, m, :]
    own_q = mine[0, m + 1, :]
    g_col = mine[:, m + 2, :]
    g_row = mine[:, m + 3, :]
    partner = owner + jnp.array([0] + offsets, jnp.int32)
    valid = jnp.logical_and(partner >= 0, partner < group)
    q_rows = lax.dynamic_slice_in_dim(own_q, widx * m, m)
    resid = q_rows[None, :, None] + q_p[:, None, :] - mine[:, :m, :]
    resid = jnp.where(valid[:, None, None], resid, jnp.zeros_like(resid))
    row_sums = n * own_q[None, :] + jnp.sum(q_p, axis=1, keepdims=True) - g_row
    col_sums = jnp.sum(own_q) + n * q_p - g_col
    row_total = jnp.sum(jnp.where(valid[:, None], row_sums, jnp.zeros_like(row_sums)), axis=0)

    received = []
    for k, e in enumerate(offsets):
        pack = jnp.concatenate([resid[k + 1], col_sums[k + 1][None, :], jnp.zeros((7, n), jnp.float32)], axis=0)
        got = shifted(pack, "batch", -e)
        received.append(got[:m])
        row_total = row_total + got[m]

    low = jnp.concatenate([resid, jnp.stack(received)], axis=0).astype(jnp.bfloat16)
    low = gathered(low, 1, 2, chip_bit)
    low = gathered(low, 2, 1, core_bit)
    low = low.reshape(low.shape[0], n, n)

    pulled = jnp.zeros(student.shape, jnp.float32)
    for k in range(tiles):
        pulled = pulled + jnp.dot(low[k], s_band[k], preferred_element_type=jnp.float32)
    for k in range(len(offsets)):
        pulled = pulled + lax.dot_general(low[tiles + k], givers[k], (((0,), (0,)), ((), ())),
                                          preferred_element_type=jnp.float32)
    grad = (student.astype(jnp.float32) * row_total[:, None] - pulled) / near_count
    return grad


def solution(mesh):
    in_specs = (P("batch", "width"), P("batch", "width"))
    out_specs = P("batch", "width")
    return jax.shard_map(body, mesh=mesh, in_specs=in_specs, out_specs=out_specs, check_vma=False)
```

```python
import jax
import jax.numpy as jnp
from jax import lax
from jax.sharding import PartitionSpec as P

REACH = 4


def shifted(block, axis, distance):
    size = lax.axis_size(axis)
    route = [(i + distance, i) for i in range(size) if 0 <= i + distance < size]
    return lax.ppermute(block, axis, route)


def swapped(block, axis, mask):
    size = lax.axis_size(axis)
    return lax.ppermute(block, axis, [(i, i ^ mask) for i in range(size)])


def split_sum(x, axis, mask, bit):
    keep = lax.dynamic_index_in_dim(x, bit, axis, keepdims=False)
    send = lax.dynamic_index_in_dim(x, 1 - bit, axis, keepdims=False)
    return keep + swapped(send, "width", mask)


def gathered(x, axis, mask, bit):
    got = swapped(x, "width", mask)
    first = jnp.where(bit == 0, x, got)
    second = jnp.where(bit == 0, got, x)
    return jnp.stack([first, second], axis=axis)


def split3(x):
    hi = lax.reduce_precision(x, exponent_bits=8, mantissa_bits=7)
    r1 = x - hi
    mid = lax.reduce_precision(r1, exponent_bits=8, mantissa_bits=7)
    lo = r1 - mid
    return jnp.stack([hi, mid, lo]).astype(jnp.bfloat16)


def join3(rows):
    rows = rows.astype(jnp.float32)
    return (rows[0] + rows[1]) + rows[2]


def pad_cols(x, cols):
    return jnp.concatenate([x, jnp.zeros((x.shape[0], cols - x.shape[1]), x.dtype)], axis=1)


def body(teacher, student):
    group = lax.axis_size("batch")
    owner = lax.axis_index("batch")
    width = lax.axis_size("width")
    widx = lax.axis_index("width")
    core_bit = widx % 2
    chip_bit = (widx // 2) % 2
    n = teacher.shape[0]
    ft = teacher.shape[1]
    fs = student.shape[1]
    dt = ft * width
    ds = fs * width
    m = n // 4
    reach = min(REACH, group - 1)
    near_count = (2 * REACH + 1) * n

    def sq(x):
        xf = x.astype(jnp.float32)
        return jnp.sum(xf * xf, axis=1)

    own_q = sq(student) / ds - sq(teacher) / dt
    zero = jnp.zeros((n,), jnp.float32)
    offsets = [d if d % 2 else -d for d in range(1, reach + 1)]
    both = jnp.concatenate([teacher, student], axis=1)
    fwd = jnp.concatenate([both, pad_cols(jnp.concatenate([split3(own_q), jnp.zeros((5, n), jnp.bfloat16)]),
                                          ft + fs)], axis=0)
    blocks = [shifted(fwd, "batch", e) for e in offsets]
    scaled = jnp.concatenate([teacher * jnp.bfloat16(-2.0 / dt), student * jnp.bfloat16(2.0 / ds)], axis=1)
    rhs = [both] + [b[:n] for b in blocks]
    q_band = [own_q] + [join3(b[n:n + 3, :n]) for b in blocks]
    s_band = [student] + [b[:n, ft:] for b in blocks]
    tiles = len(rhs)

    parts = []
    for k in range(tiles):
        g = lax.dot_general(scaled, rhs[k], (((1,), (1,)), ((), ())), preferred_element_type=jnp.float32)
        extra = jnp.stack([q_band[k], own_q if k == 0 else zero, jnp.sum(g, axis=0), jnp.sum(g, axis=1)]
                          + [zero] * 4)
        chunks = jnp.concatenate([g.reshape(4, m, n), jnp.broadcast_to(extra, (4, 8, n))], axis=1)
        parts.append(chunks.reshape(2, 2, m + 8, n))
    mine = split_sum(jnp.stack(parts), 2, 1, core_bit)
    mine = split_sum(mine, 1, 2, chip_bit)

    q_p = mine[:, m, :]
    own_q = mine[0, m + 1, :]
    g_col = mine[:, m + 2, :]
    g_row = mine[:, m + 3, :]
    partner = owner + jnp.array([0] + offsets, jnp.int32)
    valid = jnp.logical_and(partner >= 0, partner < group)
    q_rows = lax.dynamic_slice_in_dim(own_q, widx * m, m)
    resid = q_rows[None, :, None] + q_p[:, None, :] - mine[:, :m, :]
    resid = jnp.where(valid[:, None, None], resid, jnp.zeros_like(resid))
    row_sums = n * own_q[None, :] + jnp.sum(q_p, axis=1, keepdims=True) - g_row
    col_sums = jnp.sum(own_q) + n * q_p - g_col
    row_total = jnp.sum(jnp.where(valid[:, None], row_sums, jnp.zeros_like(row_sums)), axis=0)

    low_own = resid.astype(jnp.bfloat16)
    received = []
    givers = []
    for k, e in enumerate(offsets):
        pack = jnp.concatenate([low_own[k + 1], student, split3(col_sums[k + 1]), jnp.zeros((5, n), jnp.bfloat16)],
                               axis=0)
        got = shifted(pack, "batch", -e)
        received.append(got[:m])
        givers.append(got[m:m + n])
        row_total = row_total + join3(got[m + n:m + n + 3])

    low = jnp.concatenate([low_own, jnp.stack(received)], axis=0)
    low = gathered(low, 1, 2, chip_bit)
    low = gathered(low, 2, 1, core_bit)
    low = low.reshape(low.shape[0], n, n)

    pulled = jnp.zeros(student.shape, jnp.float32)
    for k in range(tiles):
        pulled = pulled + jnp.dot(low[k], s_band[k], preferred_element_type=jnp.float32)
    for k in range(len(offsets)):
        pulled = pulled + lax.dot_general(low[tiles + k], givers[k], (((0,), (0,)), ((), ())),
                                          preferred_element_type=jnp.float32)
    grad = (student.astype(jnp.float32) * row_total[:, None] - pulled) / near_count
    return grad


def solution(mesh):
    in_specs = (P("batch", "width"), P("batch", "width"))
    out_specs = P("batch", "width")
    return jax.shard_map(body, mesh=mesh, in_specs=in_specs, out_specs=out_specs, check_vma=False)
```

```python
import jax
import jax.numpy as jnp
from jax import lax
from jax.sharding import PartitionSpec as P


REACH = 4


def shifted(block, axis, distance):
    size = lax.axis_size(axis)
    route = [(i + distance, i) for i in range(size) if 0 <= i + distance < size]
    return lax.ppermute(block, axis, route)


def swapped(block, axis, mask):
    size = lax.axis_size(axis)
    return lax.ppermute(block, axis, [(i, i ^ mask) for i in range(size)])


def halves(x, axis, bit):
    half = x.shape[axis] // 2
    mine = (lax.axis_index("width") // bit) % 2
    keep = lax.dynamic_slice_in_dim(x, mine * half, half, axis)
    send = lax.dynamic_slice_in_dim(x, (1 - mine) * half, half, axis)
    return keep, send, mine


def joined(keep, got, axis, mine):
    first = jnp.where(mine == 0, keep, got)
    second = jnp.where(mine == 0, got, keep)
    return jnp.concatenate([first, second], axis=axis)


def width_sum(x):
    width = lax.axis_size("width")
    if width != 4:
        return lax.psum(x, "width")
    keep, send, core = halves(x, 2, 1)
    part = keep + swapped(send, "width", 1)
    keep, send, chip = halves(part, 1, 2)
    part = keep + swapped(send, "width", 2)
    part = joined(part, swapped(part, "width", 2), 1, chip)
    return joined(part, swapped(part, "width", 1), 2, core)


def layer(teacher, student):
    group = lax.axis_size("batch")
    owner = lax.axis_index("batch")
    width = lax.axis_size("width")
    rows_dev = teacher.shape[0]
    ft = teacher.shape[1]
    fs = student.shape[1]
    dt = ft * width
    ds = fs * width
    reach = min(REACH, group - 1)
    near_count = (2 * REACH + 1) * rows_dev

    offsets = [0] + [d if d % 2 else -d for d in range(1, reach + 1)]
    both = jnp.concatenate([teacher, student], axis=1)
    teacher_band = [teacher]
    student_band = [student]
    for e in offsets[1:]:
        got = shifted(both, "batch", e)
        teacher_band.append(got[:, :ft])
        student_band.append(got[:, ft:])

    def sq(x):
        xf = x.astype(jnp.float32)
        return jnp.sum(xf * xf, axis=1)

    def tile_part(t_d, s_d, pad):
        tg = lax.dot_general(teacher, t_d, (((1,), (1,)), ((), ())), preferred_element_type=jnp.float32)
        sg = lax.dot_general(student, s_d, (((1,), (1,)), ((), ())), preferred_element_type=jnp.float32)
        q_d = sq(s_d) / ds - sq(t_d) / dt
        return jnp.concatenate(
            [sg * (2.0 / ds) - tg * (2.0 / dt), q_d[None, :], jnp.zeros((pad, rows_dev), jnp.float32)], axis=0)

    student_f = student.astype(jnp.float32)
    row_total = jnp.zeros((rows_dev,), jnp.float32)
    pulled = jnp.zeros(student.shape, jnp.float32)
    own_q = None
    split = min(3, len(offsets))
    for group_idx in ([list(range(split)), list(range(split, len(offsets)))]):
        if not group_idx:
            continue
        pad = (-(rows_dev + 1)) % 8 + (8 if group_idx[0] else 0)
        total = width_sum(jnp.stack([tile_part(teacher_band[d], student_band[d], pad) for d in group_idx]))
        if own_q is None:
            own_q = total[0, rows_dev, :]
        for k, d in enumerate(group_idx):
            e = offsets[d]
            resid = own_q[:, None] + total[k, rows_dev, :][None, :] - total[k, :rows_dev, :]
            if d > 0:
                valid = jnp.logical_and(owner + e >= 0, owner + e < group)
                resid = jnp.where(valid, resid, jnp.zeros_like(resid))
            low = resid.astype(jnp.bfloat16)
            row_total = row_total + jnp.sum(resid, axis=1)
            pulled = pulled + jnp.dot(low, student_band[d], preferred_element_type=jnp.float32)
            if d > 0:
                back = lax.dot_general(low, student, (((0,), (0,)), ((), ())), preferred_element_type=jnp.float32)
                col = jnp.sum(resid, axis=0)
                if fs == rows_dev:
                    got = shifted(jnp.concatenate([back, col[None, :]], axis=0), "batch", -e)
                    pulled = pulled + got[:rows_dev]
                    row_total = row_total + got[rows_dev]
                else:
                    back_r, col_r = shifted((back, col), "batch", -e)
                    pulled = pulled + back_r
                    row_total = row_total + col_r
    grad = (student_f * row_total[:, None] - pulled) / near_count
    return grad


def solution(mesh):
    in_specs = (P("batch", "width"), P("batch", "width"))
    out_specs = P("batch", "width")
    return jax.shard_map(layer, mesh=mesh, in_specs=in_specs, out_specs=out_specs, check_vma=False)
```

```python
import jax
import jax.numpy as jnp
from jax import lax
from jax.sharding import PartitionSpec as P

REACH = 4


def shifted(block, axis, distance):
    size = lax.axis_size(axis)
    route = [(i + distance, i) for i in range(size) if 0 <= i + distance < size]
    return lax.ppermute(block, axis, route)


def swapped(block, axis, mask):
    size = lax.axis_size(axis)
    return lax.ppermute(block, axis, [(i, i ^ mask) for i in range(size)])


def halves(x, axis, bit):
    half = x.shape[axis] // 2
    mine = (lax.axis_index("width") // bit) % 2
    keep = lax.dynamic_slice_in_dim(x, mine * half, half, axis)
    send = lax.dynamic_slice_in_dim(x, (1 - mine) * half, half, axis)
    return keep, send, mine


def joined(keep, got, axis, mine):
    first = jnp.where(mine == 0, keep, got)
    second = jnp.where(mine == 0, got, keep)
    return jnp.concatenate([first, second], axis=axis)


def width_sum(x):
    width = lax.axis_size("width")
    if width != 4:
        return lax.psum(x, "width")
    keep, send, core = halves(x, 2, 1)
    part = keep + swapped(send, "width", 1)
    keep, send, chip = halves(part, 1, 2)
    part = keep + swapped(send, "width", 2)
    part = joined(part, swapped(part, "width", 2), 1, chip)
    return joined(part, swapped(part, "width", 1), 2, core)


def split3(x):
    hi = lax.reduce_precision(x, exponent_bits=8, mantissa_bits=7)
    r1 = x - hi
    mid = lax.reduce_precision(r1, exponent_bits=8, mantissa_bits=7)
    lo = r1 - mid
    return jnp.stack([hi, mid, lo]).astype(jnp.bfloat16)


def join3(rows):
    rows = rows.astype(jnp.float32)
    return (rows[0] + rows[1]) + rows[2]


def body(teacher, student):
    group = lax.axis_size("batch")
    owner = lax.axis_index("batch")
    width = lax.axis_size("width")
    rows_dev = teacher.shape[0]
    ft = teacher.shape[1]
    fs = student.shape[1]
    dt = ft * width
    ds = fs * width
    reach = min(REACH, group - 1)
    near_count = (2 * REACH + 1) * rows_dev

    def sq(x):
        xf = x.astype(jnp.float32)
        return jnp.sum(xf * xf, axis=1)

    own_q = sq(student) / ds - sq(teacher) / dt
    offsets = [0] + [d if d % 2 else -d for d in range(1, reach + 1)]
    both = jnp.concatenate([teacher, student], axis=1)
    q_rows = jnp.concatenate([split3(own_q), jnp.zeros((5, rows_dev), jnp.bfloat16)])
    q_rows = jnp.concatenate([q_rows, jnp.zeros((8, ft + fs - rows_dev), jnp.bfloat16)], axis=1)
    fwd = jnp.concatenate([both, q_rows], axis=0)
    scaled = jnp.concatenate([teacher * jnp.bfloat16(-2.0 / dt), student * jnp.bfloat16(2.0 / ds)], axis=1)
    rhs_band = [both]
    q_band = [own_q]
    student_band = [student]
    for e in offsets[1:]:
        got = shifted(fwd, "batch", e)
        rhs_band.append(got[:rows_dev])
        q_band.append(join3(got[rows_dev:rows_dev + 3, :rows_dev]))
        student_band.append(got[:rows_dev, ft:])

    pad = (-(rows_dev + 1)) % 8

    def tile_part(d):
        g = lax.dot_general(scaled, rhs_band[d], (((1,), (1,)), ((), ())), preferred_element_type=jnp.float32)
        return jnp.concatenate([g, q_band[d][None, :], jnp.zeros((pad, rows_dev), jnp.float32)], axis=0)

    student_f = student.astype(jnp.float32)
    row_total = jnp.zeros((rows_dev,), jnp.float32)
    pulled = jnp.zeros(student.shape, jnp.float32)
    own_q = None
    split = min(3, len(offsets))
    for group_idx in ([list(range(split)), list(range(split, len(offsets)))]):
        if not group_idx:
            continue
        total = width_sum(jnp.stack([tile_part(d) for d in group_idx]))
        if own_q is None:
            own_q = total[0, rows_dev, :]
        for k, d in enumerate(group_idx):
            e = offsets[d]
            resid = own_q[:, None] + total[k, rows_dev, :][None, :] - total[k, :rows_dev, :]
            if d > 0:
                valid = jnp.logical_and(owner + e >= 0, owner + e < group)
                resid = jnp.where(valid, resid, jnp.zeros_like(resid))
            low = resid.astype(jnp.bfloat16)
            row_total = row_total + jnp.sum(resid, axis=1)
            pulled = pulled + jnp.dot(low, student_band[d], preferred_element_type=jnp.float32)
            if d > 0:
                back = lax.dot_general(low, student, (((0,), (0,)), ((), ())), preferred_element_type=jnp.float32)
                col = jnp.sum(resid, axis=0)
                if fs == rows_dev:
                    got = shifted(jnp.concatenate([back, col[None, :]], axis=0), "batch", -e)
                    pulled = pulled + got[:rows_dev]
                    row_total = row_total + got[rows_dev]
                else:
                    back_r, col_r = shifted((back, col), "batch", -e)
                    pulled = pulled + back_r
                    row_total = row_total + col_r
    grad = (student_f * row_total[:, None] - pulled) / near_count
    return grad


def solution(mesh):
    in_specs = (P("batch", "width"), P("batch", "width"))
    out_specs = P("batch", "width")
    return jax.shard_map(body, mesh=mesh, in_specs=in_specs, out_specs=out_specs, check_vma=False)
```

```python
import jax
import jax.numpy as jnp
from jax import lax
from jax.sharding import PartitionSpec as P

REACH = 4


def shifted(block, axis, distance):
    size = lax.axis_size(axis)
    route = [(i + distance, i) for i in range(size) if 0 <= i + distance < size]
    return lax.ppermute(block, axis, route)


def swapped(block, axis, mask):
    size = lax.axis_size(axis)
    return lax.ppermute(block, axis, [(i, i ^ mask) for i in range(size)])


def halves(x, axis, bit):
    half = x.shape[axis] // 2
    mine = (lax.axis_index("width") // bit) % 2
    keep = lax.dynamic_slice_in_dim(x, mine * half, half, axis)
    send = lax.dynamic_slice_in_dim(x, (1 - mine) * half, half, axis)
    return keep, send, mine


def joined(keep, got, axis, mine):
    first = jnp.where(mine == 0, keep, got)
    second = jnp.where(mine == 0, got, keep)
    return jnp.concatenate([first, second], axis=axis)


def width_sum(x):
    width = lax.axis_size("width")
    if width != 4:
        return lax.psum(x, "width")
    keep, send, core = halves(x, 2, 1)
    part = keep + swapped(send, "width", 1)
    keep, send, chip = halves(part, 1, 2)
    part = keep + swapped(send, "width", 2)
    part = joined(part, swapped(part, "width", 2), 1, chip)
    return joined(part, swapped(part, "width", 1), 2, core)


def split3(x):
    hi = lax.reduce_precision(x, exponent_bits=8, mantissa_bits=7)
    r1 = x - hi
    mid = lax.reduce_precision(r1, exponent_bits=8, mantissa_bits=7)
    lo = r1 - mid
    return jnp.stack([hi, mid, lo]).astype(jnp.bfloat16)


def join3(rows):
    rows = rows.astype(jnp.float32)
    return (rows[0] + rows[1]) + rows[2]


def body(teacher, student):
    group = lax.axis_size("batch")
    owner = lax.axis_index("batch")
    width = lax.axis_size("width")
    rows_dev = teacher.shape[0]
    ft = teacher.shape[1]
    fs = student.shape[1]
    dt = ft * width
    ds = fs * width
    reach = min(REACH, group - 1)
    near_count = (2 * REACH + 1) * rows_dev

    def sq(x):
        xf = x.astype(jnp.float32)
        return jnp.sum(xf * xf, axis=1)

    own_q = sq(student) / ds - sq(teacher) / dt
    offsets = [0] + [d if d % 2 else -d for d in range(1, reach + 1)]
    both = jnp.concatenate([teacher, student], axis=1)
    q_rows = jnp.concatenate([split3(own_q), jnp.zeros((5, rows_dev), jnp.bfloat16)])
    q_rows = jnp.concatenate([q_rows, jnp.zeros((8, ft + fs - rows_dev), jnp.bfloat16)], axis=1)
    fwd = jnp.concatenate([both, q_rows], axis=0)
    scaled = jnp.concatenate([teacher * jnp.bfloat16(-2.0 / dt), student * jnp.bfloat16(2.0 / ds)], axis=1)
    rhs_band = [both]
    q_band = [own_q]
    student_band = [student]
    for e in offsets[1:]:
        got = shifted(fwd, "batch", e)
        rhs_band.append(got[:rows_dev])
        q_band.append(join3(got[rows_dev:rows_dev + 3, :rows_dev]))
        student_band.append(got[:rows_dev, ft:])

    pad = (-(rows_dev + 1)) % 8

    def tile_part(d):
        g = lax.dot_general(scaled, rhs_band[d], (((1,), (1,)), ((), ())), preferred_element_type=jnp.float32)
        return jnp.concatenate([g, q_band[d][None, :], jnp.zeros((pad, rows_dev), jnp.float32)], axis=0)

    student_f = student.astype(jnp.float32)
    row_total = jnp.zeros((rows_dev,), jnp.float32)
    pulled = jnp.zeros(student.shape, jnp.float32)
    own_q = None
    sizes = [2, 2, 1]
    groups = []
    for size in sizes:
        used = sum(len(g) for g in groups)
        groups.append(list(range(used, min(used + size, len(offsets)))))
    for group_idx in groups:
        if not group_idx:
            continue
        total = width_sum(jnp.stack([tile_part(d) for d in group_idx]))
        if own_q is None:
            own_q = total[0, rows_dev, :]
        for k, d in enumerate(group_idx):
            e = offsets[d]
            resid = own_q[:, None] + total[k, rows_dev, :][None, :] - total[k, :rows_dev, :]
            if d > 0:
                valid = jnp.logical_and(owner + e >= 0, owner + e < group)
                resid = jnp.where(valid, resid, jnp.zeros_like(resid))
            low = resid.astype(jnp.bfloat16)
            row_total = row_total + jnp.sum(resid, axis=1)
            pulled = pulled + jnp.dot(low, student_band[d], preferred_element_type=jnp.float32)
            if d > 0:
                back = lax.dot_general(low, student, (((0,), (0,)), ((), ())), preferred_element_type=jnp.float32)
                col = jnp.sum(resid, axis=0)
                if fs == rows_dev:
                    got = shifted(jnp.concatenate([back, col[None, :]], axis=0), "batch", -e)
                    pulled = pulled + got[:rows_dev]
                    row_total = row_total + got[rows_dev]
                else:
                    back_r, col_r = shifted((back, col), "batch", -e)
                    pulled = pulled + back_r
                    row_total = row_total + col_r
    grad = (student_f * row_total[:, None] - pulled) / near_count
    return grad


def solution(mesh):
    in_specs = (P("batch", "width"), P("batch", "width"))
    out_specs = P("batch", "width")
    return jax.shard_map(body, mesh=mesh, in_specs=in_specs, out_specs=out_specs, check_vma=False)
```

```python
import jax
import jax.numpy as jnp
from jax import lax
from jax.sharding import PartitionSpec as P

REACH = 4


def shifted(block, axis, distance):
    size = lax.axis_size(axis)
    route = [(i + distance, i) for i in range(size) if 0 <= i + distance < size]
    return lax.ppermute(block, axis, route)


def swapped(block, axis, mask):
    size = lax.axis_size(axis)
    return lax.ppermute(block, axis, [(i, i ^ mask) for i in range(size)])


def halves(x, axis, bit):
    half = x.shape[axis] // 2
    mine = (lax.axis_index("width") // bit) % 2
    keep = lax.dynamic_slice_in_dim(x, mine * half, half, axis)
    send = lax.dynamic_slice_in_dim(x, (1 - mine) * half, half, axis)
    return keep, send, mine


def joined(keep, got, axis, mine):
    first = jnp.where(mine == 0, keep, got)
    second = jnp.where(mine == 0, got, keep)
    return jnp.concatenate([first, second], axis=axis)


def width_sum(x):
    width = lax.axis_size("width")
    if width != 4:
        return lax.psum(x, "width")
    keep, send, core = halves(x, 2, 1)
    part = keep + swapped(send, "width", 1)
    keep, send, chip = halves(part, 1, 2)
    part = keep + swapped(send, "width", 2)
    part = joined(part, swapped(part, "width", 2), 1, chip)
    return joined(part, swapped(part, "width", 1), 2, core)


def split3(x):
    hi = lax.reduce_precision(x, exponent_bits=8, mantissa_bits=7)
    r1 = x - hi
    mid = lax.reduce_precision(r1, exponent_bits=8, mantissa_bits=7)
    lo = r1 - mid
    return jnp.stack([hi, mid, lo]).astype(jnp.bfloat16)


def join3(rows):
    rows = rows.astype(jnp.float32)
    return (rows[0] + rows[1]) + rows[2]


def body(teacher, student):
    group = lax.axis_size("batch")
    owner = lax.axis_index("batch")
    width = lax.axis_size("width")
    rows_dev = teacher.shape[0]
    ft = teacher.shape[1]
    fs = student.shape[1]
    dt = ft * width
    ds = fs * width
    reach = min(REACH, group - 1)
    near_count = (2 * REACH + 1) * rows_dev

    def sq(x):
        xf = x.astype(jnp.float32)
        return jnp.sum(xf * xf, axis=1)

    own_q = sq(student) / ds - sq(teacher) / dt
    offsets = [0] + [d if d % 2 else -d for d in range(1, reach + 1)]
    both = jnp.concatenate([teacher, student], axis=1)
    q_rows = jnp.concatenate([split3(own_q), jnp.zeros((5, rows_dev), jnp.bfloat16)])
    q_rows = jnp.concatenate([q_rows, jnp.zeros((8, ft + fs - rows_dev), jnp.bfloat16)], axis=1)
    fwd = jnp.concatenate([both, q_rows], axis=0)
    scaled = jnp.concatenate([teacher * jnp.bfloat16(-2.0 / dt), student * jnp.bfloat16(2.0 / ds)], axis=1)
    rhs_band = [both]
    q_band = [own_q]
    student_band = [student]
    for e in offsets[1:]:
        got = shifted(fwd, "batch", e)
        rhs_band.append(got[:rows_dev])
        q_band.append(join3(got[rows_dev:rows_dev + 3, :rows_dev]))
        student_band.append(got[:rows_dev, ft:])

    pad = (-(rows_dev + 1)) % 8

    def tile_part(d):
        g = lax.dot_general(scaled, rhs_band[d], (((1,), (1,)), ((), ())), preferred_element_type=jnp.float32)
        return jnp.concatenate([g, q_band[d][None, :], jnp.zeros((pad, rows_dev), jnp.float32)], axis=0)

    student_f = student.astype(jnp.float32)
    row_total = jnp.zeros((rows_dev,), jnp.float32)
    pulled = jnp.zeros(student.shape, jnp.float32)
    pulled_t = jnp.zeros((fs, rows_dev), jnp.float32)
    student_t = student.T
    own_q = None
    split = min(3, len(offsets))
    for group_idx in ([list(range(split)), list(range(split, len(offsets)))]):
        if not group_idx:
            continue
        total = width_sum(jnp.stack([tile_part(d) for d in group_idx]))
        if own_q is None:
            own_q = total[0, rows_dev, :]
        for k, d in enumerate(group_idx):
            e = offsets[d]
            resid = own_q[:, None] + total[k, rows_dev, :][None, :] - total[k, :rows_dev, :]
            if d > 0:
                valid = jnp.logical_and(owner + e >= 0, owner + e < group)
                resid = jnp.where(valid, resid, jnp.zeros_like(resid))
            low = resid.astype(jnp.bfloat16)
            row_total = row_total + jnp.sum(resid, axis=1)
            pulled = pulled + jnp.dot(low, student_band[d], preferred_element_type=jnp.float32)
            if d > 0:
                col = jnp.sum(resid, axis=0)
                if fs == rows_dev:
                    back_t = jnp.dot(student_t, low, preferred_element_type=jnp.float32)
                    got = shifted(jnp.concatenate([back_t, col[None, :]], axis=0), "batch", -e)
                    pulled_t = pulled_t + got[:fs]
                    row_total = row_total + got[fs]
                else:
                    back = lax.dot_general(low, student, (((0,), (0,)), ((), ())), preferred_element_type=jnp.float32)
                    back_r, col_r = shifted((back, col), "batch", -e)
                    pulled = pulled + back_r
                    row_total = row_total + col_r
    if fs == rows_dev:
        pulled = pulled + pulled_t.T
    grad = (student_f * row_total[:, None] - pulled) / near_count
    return grad


def solution(mesh):
    in_specs = (P("batch", "width"), P("batch", "width"))
    out_specs = P("batch", "width")
    return jax.shard_map(body, mesh=mesh, in_specs=in_specs, out_specs=out_specs, check_vma=False)
```

```python
import jax
import jax.numpy as jnp
from jax import lax
from jax.sharding import PartitionSpec as P


REACH = 4


def shifted(block, axis, distance):
    size = lax.axis_size(axis)
    route = [(i + distance, i) for i in range(size) if 0 <= i + distance < size]
    return lax.ppermute(block, axis, route)


def swapped(block, axis, mask):
    size = lax.axis_size(axis)
    return lax.ppermute(block, axis, [(i, i ^ mask) for i in range(size)])


def halves(x, axis, bit):
    half = x.shape[axis] // 2
    mine = (lax.axis_index("width") // bit) % 2
    keep = lax.dynamic_slice_in_dim(x, mine * half, half, axis)
    send = lax.dynamic_slice_in_dim(x, (1 - mine) * half, half, axis)
    return keep, send, mine


def joined(keep, got, axis, mine):
    first = jnp.where(mine == 0, keep, got)
    second = jnp.where(mine == 0, got, keep)
    return jnp.concatenate([first, second], axis=axis)


def width_sum(x):
    width = lax.axis_size("width")
    if width != 4:
        return lax.psum(x, "width")
    keep, send, core = halves(x, 2, 1)
    part = keep + swapped(send, "width", 1)
    keep, send, chip = halves(part, 1, 2)
    part = keep + swapped(send, "width", 2)
    part = joined(part, swapped(part, "width", 2), 1, chip)
    return joined(part, swapped(part, "width", 1), 2, core)


def split3(x):
    hi = lax.reduce_precision(x, exponent_bits=8, mantissa_bits=7)
    r1 = x - hi
    mid = lax.reduce_precision(r1, exponent_bits=8, mantissa_bits=7)
    lo = r1 - mid
    return jnp.stack([hi, mid, lo]).astype(jnp.bfloat16)


def join3(rows):
    rows = rows.astype(jnp.float32)
    return (rows[0] + rows[1]) + rows[2]


def layer(teacher, student):
    group = lax.axis_size("batch")
    owner = lax.axis_index("batch")
    width = lax.axis_size("width")
    rows_dev = teacher.shape[0]
    ft = teacher.shape[1]
    fs = student.shape[1]
    dt = ft * width
    ds = fs * width
    reach = min(REACH, group - 1)
    near_count = (2 * REACH + 1) * rows_dev

    def sq(x):
        xf = x.astype(jnp.float32)
        return jnp.sum(xf * xf, axis=1)

    own_q = sq(student) / ds - sq(teacher) / dt
    offsets = [0] + [d if d % 2 else -d for d in range(1, reach + 1)]
    both = jnp.concatenate([teacher, student], axis=1)
    q_rows = jnp.concatenate([split3(own_q), jnp.zeros((5, rows_dev), jnp.bfloat16)])
    q_rows = jnp.concatenate([q_rows, jnp.zeros((8, ft + fs - rows_dev), jnp.bfloat16)], axis=1)
    fwd = jnp.concatenate([both, q_rows], axis=0)
    scaled = jnp.concatenate([teacher * jnp.bfloat16(-2.0 / dt), student * jnp.bfloat16(2.0 / ds)], axis=1)
    rhs_band = [both]
    q_band = [own_q]
    student_band = [student]
    for e in offsets[1:]:
        got = shifted(fwd, "batch", e)
        rhs_band.append(got[:rows_dev])
        q_band.append(join3(got[rows_dev:rows_dev + 3, :rows_dev]))
        student_band.append(got[:rows_dev, ft:])

    pad = (-(rows_dev + 1)) % 8

    def tile_part(d, near):
        g = lax.dot_general(scaled, rhs_band[d], (((1,), (1,)), ((), ())), preferred_element_type=jnp.float32)
        rows = jnp.zeros((pad + (0 if near else 8), rows_dev), jnp.float32)
        return jnp.concatenate([g, q_band[d][None, :], rows], axis=0)

    student_f = student.astype(jnp.float32)
    row_total = jnp.zeros((rows_dev,), jnp.float32)
    pulled = jnp.zeros(student.shape, jnp.float32)
    own_q = None
    split = min(3, len(offsets))
    for group_idx in ([list(range(split)), list(range(split, len(offsets)))]):
        if not group_idx:
            continue
        near = group_idx[0] == 0
        total = width_sum(jnp.stack([tile_part(d, near) for d in group_idx]))
        if own_q is None:
            own_q = total[0, rows_dev, :]
        for k, d in enumerate(group_idx):
            e = offsets[d]
            resid = own_q[:, None] + total[k, rows_dev, :][None, :] - total[k, :rows_dev, :]
            if d > 0:
                valid = jnp.logical_and(owner + e >= 0, owner + e < group)
                resid = jnp.where(valid, resid, jnp.zeros_like(resid))
            low = resid.astype(jnp.bfloat16)
            row_total = row_total + jnp.sum(resid, axis=1)
            pulled = pulled + jnp.dot(low, student_band[d], preferred_element_type=jnp.float32)
            if d > 0:
                back = lax.dot_general(low, student, (((0,), (0,)), ((), ())), preferred_element_type=jnp.float32)
                col = jnp.sum(resid, axis=0)
                if fs == rows_dev:
                    got = shifted(jnp.concatenate([back, col[None, :]], axis=0), "batch", -e)
                    pulled = pulled + got[:rows_dev]
                    row_total = row_total + got[rows_dev]
                else:
                    back_r, col_r = shifted((back, col), "batch", -e)
                    pulled = pulled + back_r
                    row_total = row_total + col_r
    grad = (student_f * row_total[:, None] - pulled) / near_count
    return grad


def solution(mesh):
    in_specs = (P("batch", "width"), P("batch", "width"))
    out_specs = P("batch", "width")
    return jax.shard_map(layer, mesh=mesh, in_specs=in_specs, out_specs=out_specs, check_vma=False)
```

```python
import jax
import jax.numpy as jnp
from jax import lax
from jax.sharding import PartitionSpec as P


REACH = 4


def shifted(block, axis, distance):
    size = lax.axis_size(axis)
    route = [(i + distance, i) for i in range(size) if 0 <= i + distance < size]
    return lax.ppermute(block, axis, route)


def swapped(block, axis, mask):
    size = lax.axis_size(axis)
    return lax.ppermute(block, axis, [(i, i ^ mask) for i in range(size)])


def halves(x, axis, bit):
    half = x.shape[axis] // 2
    mine = (lax.axis_index("width") // bit) % 2
    keep = lax.dynamic_slice_in_dim(x, mine * half, half, axis)
    send = lax.dynamic_slice_in_dim(x, (1 - mine) * half, half, axis)
    return keep, send, mine


def joined(keep, got, axis, mine):
    first = jnp.where(mine == 0, keep, got)
    second = jnp.where(mine == 0, got, keep)
    return jnp.concatenate([first, second], axis=axis)


def width_sum(x):
    width = lax.axis_size("width")
    if width != 4:
        return lax.psum(x, "width")
    keep, send, core = halves(x, 2, 1)
    part = keep + swapped(send, "width", 1)
    keep, send, chip = halves(part, 1, 2)
    part = keep + swapped(send, "width", 2)
    part = joined(part, swapped(part, "width", 2), 1, chip)
    return joined(part, swapped(part, "width", 1), 2, core)


def split3(x):
    hi = lax.reduce_precision(x, exponent_bits=8, mantissa_bits=7)
    r1 = x - hi
    mid = lax.reduce_precision(r1, exponent_bits=8, mantissa_bits=7)
    lo = r1 - mid
    return jnp.stack([hi, mid, lo]).astype(jnp.bfloat16)


def join3(rows):
    rows = rows.astype(jnp.float32)
    return (rows[0] + rows[1]) + rows[2]


def layer(teacher, student):
    group = lax.axis_size("batch")
    owner = lax.axis_index("batch")
    width = lax.axis_size("width")
    rows_dev = teacher.shape[0]
    ft = teacher.shape[1]
    fs = student.shape[1]
    dt = ft * width
    ds = fs * width
    reach = min(REACH, group - 1)
    near_count = (2 * REACH + 1) * rows_dev

    def sq(x):
        xf = x.astype(jnp.float32)
        return jnp.sum(xf * xf, axis=1)

    own_q = sq(student) / ds - sq(teacher) / dt
    offsets = [0] + [d if d % 2 else -d for d in range(1, reach + 1)]
    both = jnp.concatenate([teacher, student], axis=1)
    q_rows = jnp.concatenate([split3(own_q), jnp.zeros((5, rows_dev), jnp.bfloat16)])
    q_rows = jnp.concatenate([q_rows, jnp.zeros((8, ft + fs - rows_dev), jnp.bfloat16)], axis=1)
    fwd = jnp.concatenate([both, q_rows], axis=0)
    scaled = jnp.concatenate([teacher * jnp.bfloat16(-2.0 / dt), student * jnp.bfloat16(2.0 / ds)], axis=1)
    rhs_band = [both]
    q_band = [own_q]
    student_band = [student]
    for e in offsets[1:]:
        got = shifted(fwd, "batch", e)
        rhs_band.append(got[:rows_dev])
        q_band.append(join3(got[rows_dev:rows_dev + 3, :rows_dev]))
        student_band.append(got[:rows_dev, ft:])

    pad = (-(rows_dev + 1)) % 8

    def tile_part(d):
        g = lax.dot_general(scaled, rhs_band[d], (((1,), (1,)), ((), ())), preferred_element_type=jnp.float32)
        rows = jnp.zeros((pad + (8 if d == 0 else 16 if d >= 3 else 0), rows_dev), jnp.float32)
        return jnp.concatenate([g, q_band[d][None, :], rows], axis=0)

    student_f = student.astype(jnp.float32)
    row_total = jnp.zeros((rows_dev,), jnp.float32)
    pulled = jnp.zeros(student.shape, jnp.float32)
    own_q = None
    split = min(3, len(offsets))
    for group_idx in ([[0], list(range(1, split)), list(range(split, len(offsets)))]):
        if not group_idx:
            continue
        total = width_sum(jnp.stack([tile_part(d) for d in group_idx]))
        if own_q is None:
            own_q = total[0, rows_dev, :]
        for k, d in enumerate(group_idx):
            e = offsets[d]
            resid = own_q[:, None] + total[k, rows_dev, :][None, :] - total[k, :rows_dev, :]
            if d > 0:
                valid = jnp.logical_and(owner + e >= 0, owner + e < group)
                resid = jnp.where(valid, resid, jnp.zeros_like(resid))
            low = resid.astype(jnp.bfloat16)
            row_total = row_total + jnp.sum(resid, axis=1)
            pulled = pulled + jnp.dot(low, student_band[d], preferred_element_type=jnp.float32)
            if d > 0:
                back = lax.dot_general(low, student, (((0,), (0,)), ((), ())), preferred_element_type=jnp.float32)
                col = jnp.sum(resid, axis=0)
                if fs == rows_dev:
                    got = shifted(jnp.concatenate([back, col[None, :]], axis=0), "batch", -e)
                    pulled = pulled + got[:rows_dev]
                    row_total = row_total + got[rows_dev]
                else:
                    back_r, col_r = shifted((back, col), "batch", -e)
                    pulled = pulled + back_r
                    row_total = row_total + col_r
    grad = (student_f * row_total[:, None] - pulled) / near_count
    return grad


def solution(mesh):
    in_specs = (P("batch", "width"), P("batch", "width"))
    out_specs = P("batch", "width")
    return jax.shard_map(layer, mesh=mesh, in_specs=in_specs, out_specs=out_specs, check_vma=False)
```

```python
import jax
import jax.numpy as jnp
from jax import lax
from jax.sharding import PartitionSpec as P


REACH = 4


def shifted(block, axis, distance):
    size = lax.axis_size(axis)
    route = [(i + distance, i) for i in range(size) if 0 <= i + distance < size]
    return lax.ppermute(block, axis, route)


def swapped(block, axis, mask):
    size = lax.axis_size(axis)
    return lax.ppermute(block, axis, [(i, i ^ mask) for i in range(size)])


def halves(x, axis, bit):
    half = x.shape[axis] // 2
    mine = (lax.axis_index("width") // bit) % 2
    keep = lax.dynamic_slice_in_dim(x, mine * half, half, axis)
    send = lax.dynamic_slice_in_dim(x, (1 - mine) * half, half, axis)
    return keep, send, mine


def joined(keep, got, axis, mine):
    first = jnp.where(mine == 0, keep, got)
    second = jnp.where(mine == 0, got, keep)
    return jnp.concatenate([first, second], axis=axis)


def width_sum(x):
    width = lax.axis_size("width")
    if width != 4:
        return lax.psum(x, "width")
    keep, send, core = halves(x, 2, 1)
    part = keep + swapped(send, "width", 1)
    keep, send, chip = halves(part, 1, 2)
    part = keep + swapped(send, "width", 2)
    part = joined(part, swapped(part, "width", 2), 1, chip)
    return joined(part, swapped(part, "width", 1), 2, core)


def layer(teacher, student):
    group = lax.axis_size("batch")
    owner = lax.axis_index("batch")
    width = lax.axis_size("width")
    rows_dev = teacher.shape[0]
    ft = teacher.shape[1]
    fs = student.shape[1]
    dt = ft * width
    ds = fs * width
    reach = min(REACH, group - 1)
    near_count = (2 * REACH + 1) * rows_dev

    def sq(x):
        xf = x.astype(jnp.float32)
        return jnp.sum(xf * xf, axis=1)

    offsets = [0] + [d if d % 2 else -d for d in range(1, reach + 1)]
    both = jnp.concatenate([teacher, student], axis=1)
    rhs_band = [both]
    for e in offsets[1:]:
        rhs_band.append(shifted(both, "batch", e))
    scaled = jnp.concatenate([teacher * jnp.bfloat16(-2.0 / dt), student * jnp.bfloat16(2.0 / ds)], axis=1)
    q_band = [sq(b[:, ft:]) / ds - sq(b[:, :ft]) / dt for b in rhs_band]
    student_band = [b[:, ft:] for b in rhs_band]

    pad = (-(rows_dev + 1)) % 8

    def tile_part(d):
        g = lax.dot_general(scaled, rhs_band[d], (((1,), (1,)), ((), ())), preferred_element_type=jnp.float32)
        rows = jnp.zeros((pad + (8 if d == 0 else 0), rows_dev), jnp.float32)
        return jnp.concatenate([g, q_band[d][None, :], rows], axis=0)

    student_f = student.astype(jnp.float32)
    row_total = jnp.zeros((rows_dev,), jnp.float32)
    pulled = jnp.zeros(student.shape, jnp.float32)
    own_q = None
    split = min(3, len(offsets))
    for group_idx in ([[0], list(range(1, split)), list(range(split, len(offsets)))]):
        if not group_idx:
            continue
        total = width_sum(jnp.stack([tile_part(d) for d in group_idx]))
        if own_q is None:
            own_q = total[0, rows_dev, :]
        for k, d in enumerate(group_idx):
            e = offsets[d]
            resid = own_q[:, None] + total[k, rows_dev, :][None, :] - total[k, :rows_dev, :]
            if d > 0:
                valid = jnp.logical_and(owner + e >= 0, owner + e < group)
                resid = jnp.where(valid, resid, jnp.zeros_like(resid))
            low = resid.astype(jnp.bfloat16)
            row_total = row_total + jnp.sum(resid, axis=1)
            pulled = pulled + jnp.dot(low, student_band[d], preferred_element_type=jnp.float32)
            if d > 0:
                back = lax.dot_general(low, student, (((0,), (0,)), ((), ())), preferred_element_type=jnp.float32)
                col = jnp.sum(resid, axis=0)
                if fs == rows_dev:
                    got = shifted(jnp.concatenate([back, col[None, :]], axis=0), "batch", -e)
                    pulled = pulled + got[:rows_dev]
                    row_total = row_total + got[rows_dev]
                else:
                    back_r, col_r = shifted((back, col), "batch", -e)
                    pulled = pulled + back_r
                    row_total = row_total + col_r
    grad = (student_f * row_total[:, None] - pulled) / near_count
    return grad


def solution(mesh):
    in_specs = (P("batch", "width"), P("batch", "width"))
    out_specs = P("batch", "width")
    return jax.shard_map(layer, mesh=mesh, in_specs=in_specs, out_specs=out_specs, check_vma=False)
```

```python
import jax
import jax.numpy as jnp
from jax import lax
from jax.sharding import PartitionSpec as P


REACH = 4


def shifted(block, axis, distance):
    size = lax.axis_size(axis)
    route = [(i + distance, i) for i in range(size) if 0 <= i + distance < size]
    return lax.ppermute(block, axis, route)


def swapped(block, axis, mask):
    size = lax.axis_size(axis)
    return lax.ppermute(block, axis, [(i, i ^ mask) for i in range(size)])


def halves(x, axis, bit):
    half = x.shape[axis] // 2
    mine = (lax.axis_index("width") // bit) % 2
    keep = lax.dynamic_slice_in_dim(x, mine * half, half, axis)
    send = lax.dynamic_slice_in_dim(x, (1 - mine) * half, half, axis)
    return keep, send, mine


def joined(keep, got, axis, mine):
    first = jnp.where(mine == 0, keep, got)
    second = jnp.where(mine == 0, got, keep)
    return jnp.concatenate([first, second], axis=axis)


def width_sum(x):
    width = lax.axis_size("width")
    if width != 4:
        return lax.psum(x, "width")
    keep, send, core = halves(x, 2, 1)
    part = keep + swapped(send, "width", 1)
    keep, send, chip = halves(part, 1, 2)
    part = keep + swapped(send, "width", 2)
    part = joined(part, swapped(part, "width", 2), 1, chip)
    return joined(part, swapped(part, "width", 1), 2, core)


def layer(teacher, student):
    group = lax.axis_size("batch")
    owner = lax.axis_index("batch")
    width = lax.axis_size("width")
    rows_dev = teacher.shape[0]
    ft = teacher.shape[1]
    fs = student.shape[1]
    dt = ft * width
    ds = fs * width
    reach = min(REACH, group - 1)
    near_count = (2 * REACH + 1) * rows_dev

    def sq(x):
        xf = x.astype(jnp.float32)
        return jnp.sum(xf * xf, axis=1)

    offsets = [0] + [d if d % 2 else -d for d in range(1, reach + 1)]
    scaled = jnp.concatenate([teacher * jnp.bfloat16(-2.0 / dt), student * jnp.bfloat16(2.0 / ds)], axis=1)
    rhs_band = [scaled]
    for e in offsets[1:]:
        rhs_band.append(shifted(scaled, "batch", e))
    both = jnp.concatenate([teacher, student], axis=1)
    q_band = [sq(student) / ds - sq(teacher) / dt]
    q_band += [sq(b[:, ft:]) * (ds / 4.0) - sq(b[:, :ft]) * (dt / 4.0) for b in rhs_band[1:]]
    student_band = [student] + [b[:, ft:] for b in rhs_band[1:]]

    pad = (-(rows_dev + 1)) % 8

    def tile_part(d):
        g = lax.dot_general(both, rhs_band[d], (((1,), (1,)), ((), ())), preferred_element_type=jnp.float32)
        rows = jnp.zeros((pad + (8 if d == 0 else 0), rows_dev), jnp.float32)
        return jnp.concatenate([g, q_band[d][None, :], rows], axis=0)

    student_f = student.astype(jnp.float32)
    row_total = jnp.zeros((rows_dev,), jnp.float32)
    pulled = jnp.zeros(student.shape, jnp.float32)
    pulled_band = jnp.zeros(student.shape, jnp.float32)
    pulled_t = jnp.zeros((fs, rows_dev), jnp.float32)
    student_t = student.T
    own_q = None
    split = min(3, len(offsets))
    for group_idx in ([[0], list(range(1, split)), list(range(split, len(offsets)))]):
        if not group_idx:
            continue
        total = width_sum(jnp.stack([tile_part(d) for d in group_idx]))
        if own_q is None:
            own_q = total[0, rows_dev, :]
        for k, d in enumerate(group_idx):
            e = offsets[d]
            resid = own_q[:, None] + total[k, rows_dev, :][None, :] - total[k, :rows_dev, :]
            if d > 0:
                valid = jnp.logical_and(owner + e >= 0, owner + e < group)
                resid = jnp.where(valid, resid, jnp.zeros_like(resid))
            low = resid.astype(jnp.bfloat16)
            row_total = row_total + jnp.sum(resid, axis=1)
            if d == 0:
                pulled = pulled + jnp.dot(low, student_band[d], preferred_element_type=jnp.float32)
            else:
                pulled_band = pulled_band + jnp.dot(low, student_band[d], preferred_element_type=jnp.float32)
            if d > 0:
                col = jnp.sum(resid, axis=0)
                if fs == rows_dev:
                    back_t = jnp.dot(student_t, low, preferred_element_type=jnp.float32)
                    got = shifted(jnp.concatenate([back_t, col[None, :]], axis=0), "batch", -e)
                    pulled_t = pulled_t + got[:fs]
                    row_total = row_total + got[fs]
                else:
                    back = lax.dot_general(low, student, (((0,), (0,)), ((), ())), preferred_element_type=jnp.float32)
                    back_r, col_r = shifted((back, col), "batch", -e)
                    pulled = pulled + back_r
                    row_total = row_total + col_r
    pulled = pulled + pulled_band * (ds / 2.0)
    if fs == rows_dev:
        pulled = pulled + pulled_t.T
    grad = (student_f * row_total[:, None] - pulled) / near_count
    return grad


def solution(mesh):
    in_specs = (P("batch", "width"), P("batch", "width"))
    out_specs = P("batch", "width")
    return jax.shard_map(layer, mesh=mesh, in_specs=in_specs, out_specs=out_specs, check_vma=False)
```

```python
import jax
import jax.numpy as jnp
from jax import lax
from jax.experimental import pallas as pl
from jax.sharding import PartitionSpec as P


REACH = 4


def shifted(block, axis, distance):
    size = lax.axis_size(axis)
    route = [(i + distance, i) for i in range(size) if 0 <= i + distance < size]
    return lax.ppermute(block, axis, route)


def swapped(block, axis, mask):
    size = lax.axis_size(axis)
    return lax.ppermute(block, axis, [(i, i ^ mask) for i in range(size)])


def halves(x, axis, bit):
    half = x.shape[axis] // 2
    mine = (lax.axis_index("width") // bit) % 2
    keep = lax.dynamic_slice_in_dim(x, mine * half, half, axis)
    send = lax.dynamic_slice_in_dim(x, (1 - mine) * half, half, axis)
    return keep, send, mine


def joined(keep, got, axis, mine):
    first = jnp.where(mine == 0, keep, got)
    second = jnp.where(mine == 0, got, keep)
    return jnp.concatenate([first, second], axis=axis)


def width_sum(x):
    width = lax.axis_size("width")
    if width != 4:
        return lax.psum(x, "width")
    keep, send, core = halves(x, 2, 1)
    part = keep + swapped(send, "width", 1)
    keep, send, chip = halves(part, 1, 2)
    part = keep + swapped(send, "width", 2)
    part = joined(part, swapped(part, "width", 2), 1, chip)
    return joined(part, swapped(part, "width", 1), 2, core)


def scaled_concat(teacher, student, t_scale, s_scale):
    rows, ft = teacher.shape
    fs = student.shape[1]
    block = 128 if rows % 128 == 0 else rows

    def kernel(t_ref, s_ref, o_ref):
        o_ref[:, :ft] = t_ref[...] * jnp.bfloat16(t_scale)
        o_ref[:, ft:] = s_ref[...] * jnp.bfloat16(s_scale)

    return pl.pallas_call(
        kernel,
        out_shape=jax.ShapeDtypeStruct((rows, ft + fs), teacher.dtype),
        grid=(rows // block,),
        in_specs=[pl.BlockSpec((block, ft), lambda i: (i, 0)), pl.BlockSpec((block, fs), lambda i: (i, 0))],
        out_specs=pl.BlockSpec((block, ft + fs), lambda i: (i, 0)),
        cost_estimate=pl.CostEstimate(flops=rows * (ft + fs), transcendentals=0,
                                      bytes_accessed=4 * rows * (ft + fs)),
    )(teacher, student)


def layer(teacher, student):
    group = lax.axis_size("batch")
    owner = lax.axis_index("batch")
    width = lax.axis_size("width")
    rows_dev = teacher.shape[0]
    ft = teacher.shape[1]
    fs = student.shape[1]
    dt = ft * width
    ds = fs * width
    reach = min(REACH, group - 1)
    near_count = (2 * REACH + 1) * rows_dev

    def sq(x):
        xf = x.astype(jnp.float32)
        return jnp.sum(xf * xf, axis=1)

    offsets = [0] + [d if d % 2 else -d for d in range(1, reach + 1)]
    scaled = scaled_concat(teacher, student, -2.0 / dt, 2.0 / ds)
    rhs_band = [scaled]
    for e in offsets[1:]:
        rhs_band.append(shifted(scaled, "batch", e))
    both = jnp.concatenate([teacher, student], axis=1)
    q_band = [sq(student) / ds - sq(teacher) / dt]
    q_band += [sq(b[:, ft:]) * (ds / 4.0) - sq(b[:, :ft]) * (dt / 4.0) for b in rhs_band[1:]]
    student_band = [student] + [b[:, ft:] for b in rhs_band[1:]]

    pad = (-(rows_dev + 1)) % 8

    def tile_part(d):
        g = lax.dot_general(both, rhs_band[d], (((1,), (1,)), ((), ())), preferred_element_type=jnp.float32)
        rows = jnp.zeros((pad + (8 if d == 0 else 0), rows_dev), jnp.float32)
        return jnp.concatenate([g, q_band[d][None, :], rows], axis=0)

    student_f = student.astype(jnp.float32)
    row_total = jnp.zeros((rows_dev,), jnp.float32)
    pulled = jnp.zeros(student.shape, jnp.float32)
    pulled_band = jnp.zeros(student.shape, jnp.float32)
    own_q = None
    split = min(3, len(offsets))
    for group_idx in ([[0], list(range(1, split)), list(range(split, len(offsets)))]):
        if not group_idx:
            continue
        total = width_sum(jnp.stack([tile_part(d) for d in group_idx]))
        if own_q is None:
            own_q = total[0, rows_dev, :]
        for k, d in enumerate(group_idx):
            e = offsets[d]
            resid = own_q[:, None] + total[k, rows_dev, :][None, :] - total[k, :rows_dev, :]
            if d > 0:
                valid = jnp.logical_and(owner + e >= 0, owner + e < group)
                resid = jnp.where(valid, resid, jnp.zeros_like(resid))
            low = resid.astype(jnp.bfloat16)
            row_total = row_total + jnp.sum(resid, axis=1)
            if d == 0:
                pulled = pulled + jnp.dot(low, student_band[d], preferred_element_type=jnp.float32)
            else:
                pulled_band = pulled_band + jnp.dot(low, student_band[d], preferred_element_type=jnp.float32)
            if d > 0:
                back = lax.dot_general(low, student, (((0,), (0,)), ((), ())), preferred_element_type=jnp.float32)
                col = jnp.sum(resid, axis=0)
                if fs == rows_dev:
                    got = shifted(jnp.concatenate([back, col[None, :]], axis=0), "batch", -e)
                    pulled = pulled + got[:rows_dev]
                    row_total = row_total + got[rows_dev]
                else:
                    back_r, col_r = shifted((back, col), "batch", -e)
                    pulled = pulled + back_r
                    row_total = row_total + col_r
    pulled = pulled + pulled_band * (ds / 2.0)
    grad = (student_f * row_total[:, None] - pulled) / near_count
    return grad


def solution(mesh):
    in_specs = (P("batch", "width"), P("batch", "width"))
    out_specs = P("batch", "width")
    return jax.shard_map(layer, mesh=mesh, in_specs=in_specs, out_specs=out_specs, check_vma=False)
```

```python
import jax
import jax.numpy as jnp
from jax import lax
from jax.sharding import PartitionSpec as P


REACH = 4


def shifted(block, axis, distance):
    size = lax.axis_size(axis)
    route = [(i + distance, i) for i in range(size) if 0 <= i + distance < size]
    return lax.ppermute(block, axis, route)


def swapped(block, axis, mask):
    size = lax.axis_size(axis)
    return lax.ppermute(block, axis, [(i, i ^ mask) for i in range(size)])


def halves(x, axis, bit):
    half = x.shape[axis] // 2
    mine = (lax.axis_index("width") // bit) % 2
    keep = lax.dynamic_slice_in_dim(x, mine * half, half, axis)
    send = lax.dynamic_slice_in_dim(x, (1 - mine) * half, half, axis)
    return keep, send, mine


def joined(keep, got, axis, mine):
    first = jnp.where(mine == 0, keep, got)
    second = jnp.where(mine == 0, got, keep)
    return jnp.concatenate([first, second], axis=axis)


def width_sum(x):
    width = lax.axis_size("width")
    if width != 4:
        return lax.psum(x, "width")
    keep, send, core = halves(x, 2, 1)
    part = keep + swapped(send, "width", 1)
    keep, send, chip = halves(part, 1, 2)
    part = keep + swapped(send, "width", 2)
    part = joined(part, swapped(part, "width", 2), 1, chip)
    return joined(part, swapped(part, "width", 1), 2, core)


def layer(teacher, student):
    group = lax.axis_size("batch")
    owner = lax.axis_index("batch")
    width = lax.axis_size("width")
    rows_dev = teacher.shape[0]
    ft = teacher.shape[1]
    fs = student.shape[1]
    dt = ft * width
    ds = fs * width
    reach = min(REACH, group - 1)
    near_count = (2 * REACH + 1) * rows_dev

    def sq(x):
        xf = x.astype(jnp.float32)
        return jnp.sum(xf * xf, axis=1)

    offsets = [0] + [d if d % 2 else -d for d in range(1, reach + 1)]
    scaled = jnp.concatenate([teacher * jnp.bfloat16(-2.0 / dt), student * jnp.bfloat16(2.0 / ds)], axis=1)
    rhs_band = [scaled]
    for e in offsets[1:]:
        rhs_band.append(shifted(scaled, "batch", e))
    both = jnp.concatenate([teacher, student], axis=1)
    q_band = [sq(student) / ds - sq(teacher) / dt]
    q_band += [sq(b[:, ft:]) * (ds / 4.0) - sq(b[:, :ft]) * (dt / 4.0) for b in rhs_band[1:]]
    student_band = [student] + [b[:, ft:] for b in rhs_band[1:]]

    pad = (-(rows_dev + 1)) % 8

    def tile_part(d):
        g = lax.dot_general(both, rhs_band[d], (((1,), (1,)), ((), ())), preferred_element_type=jnp.float32)
        rows = jnp.zeros((pad + (8 if d == 0 else 0), rows_dev), jnp.float32)
        return jnp.concatenate([g, q_band[d][None, :], rows], axis=0)

    student_f = student.astype(jnp.float32)
    row_total = jnp.zeros((rows_dev,), jnp.float32)
    pulled = jnp.zeros(student.shape, jnp.float32)
    pulled_band = jnp.zeros(student.shape, jnp.float32)
    own_q = None
    pulls = [d for d in range(1, len(offsets)) if offsets[d] > 0]
    pushes = [d for d in range(1, len(offsets)) if offsets[d] < 0]
    for group_idx in ([[0], pulls, pushes]):
        if not group_idx:
            continue
        total = width_sum(jnp.stack([tile_part(d) for d in group_idx]))
        if own_q is None:
            own_q = total[0, rows_dev, :]
        for k, d in enumerate(group_idx):
            e = offsets[d]
            resid = own_q[:, None] + total[k, rows_dev, :][None, :] - total[k, :rows_dev, :]
            if d > 0:
                valid = jnp.logical_and(owner + e >= 0, owner + e < group)
                resid = jnp.where(valid, resid, jnp.zeros_like(resid))
            low = resid.astype(jnp.bfloat16)
            row_total = row_total + jnp.sum(resid, axis=1)
            if d == 0:
                pulled = pulled + jnp.dot(low, student_band[d], preferred_element_type=jnp.float32)
            else:
                pulled_band = pulled_band + jnp.dot(low, student_band[d], preferred_element_type=jnp.float32)
            if d > 0:
                back = lax.dot_general(low, student, (((0,), (0,)), ((), ())), preferred_element_type=jnp.float32)
                col = jnp.sum(resid, axis=0)
                if fs == rows_dev:
                    got = shifted(jnp.concatenate([back, col[None, :]], axis=0), "batch", -e)
                    pulled = pulled + got[:rows_dev]
                    row_total = row_total + got[rows_dev]
                else:
                    back_r, col_r = shifted((back, col), "batch", -e)
                    pulled = pulled + back_r
                    row_total = row_total + col_r
    pulled = pulled + pulled_band * (ds / 2.0)
    grad = (student_f * row_total[:, None] - pulled) / near_count
    return grad


def solution(mesh):
    in_specs = (P("batch", "width"), P("batch", "width"))
    out_specs = P("batch", "width")
    return jax.shard_map(layer, mesh=mesh, in_specs=in_specs, out_specs=out_specs, check_vma=False)
```

```python
import jax
import jax.numpy as jnp
from jax import lax
from jax.sharding import PartitionSpec as P


REACH = 4


def shifted(block, axis, distance):
    size = lax.axis_size(axis)
    route = [(i + distance, i) for i in range(size) if 0 <= i + distance < size]
    return lax.ppermute(block, axis, route)


def swapped(block, axis, mask):
    size = lax.axis_size(axis)
    return lax.ppermute(block, axis, [(i, i ^ mask) for i in range(size)])


def halves(x, axis, bit):
    half = x.shape[axis] // 2
    mine = (lax.axis_index("width") // bit) % 2
    keep = lax.dynamic_slice_in_dim(x, mine * half, half, axis)
    send = lax.dynamic_slice_in_dim(x, (1 - mine) * half, half, axis)
    return keep, send, mine


def joined(keep, got, axis, mine):
    first = jnp.where(mine == 0, keep, got)
    second = jnp.where(mine == 0, got, keep)
    return jnp.concatenate([first, second], axis=axis)


def width_sum(x):
    width = lax.axis_size("width")
    if width != 4:
        return lax.psum(x, "width")
    keep, send, core = halves(x, 2, 1)
    part = keep + swapped(send, "width", 1)
    keep, send, chip = halves(part, 1, 2)
    part = keep + swapped(send, "width", 2)
    part = joined(part, swapped(part, "width", 2), 1, chip)
    return joined(part, swapped(part, "width", 1), 2, core)


def layer(teacher, student):
    group = lax.axis_size("batch")
    owner = lax.axis_index("batch")
    width = lax.axis_size("width")
    rows_dev = teacher.shape[0]
    ft = teacher.shape[1]
    fs = student.shape[1]
    dt = ft * width
    ds = fs * width
    reach = min(REACH, group - 1)
    near_count = (2 * REACH + 1) * rows_dev

    def sq(x):
        xf = x.astype(jnp.float32)
        return jnp.sum(xf * xf, axis=1)

    offsets = [0] + [d if d % 2 else -d for d in range(1, reach + 1)]
    scaled = jnp.concatenate([teacher * jnp.bfloat16(-2.0 / dt), student * jnp.bfloat16(2.0 / ds)], axis=1)
    rhs_band = [scaled]
    for e in offsets[1:]:
        rhs_band.append(shifted(scaled, "batch", e))
    both = jnp.concatenate([teacher, student], axis=1)
    q_band = [sq(student) / ds - sq(teacher) / dt]
    q_band += [sq(b[:, ft:]) * (ds / 4.0) - sq(b[:, :ft]) * (dt / 4.0) for b in rhs_band[1:]]
    student_band = [student] + [b[:, ft:] for b in rhs_band[1:]]

    pad = (-(rows_dev + 1)) % 8

    def tile_part(d):
        g = lax.dot_general(both, rhs_band[d], (((1,), (1,)), ((), ())), preferred_element_type=jnp.float32)
        rows = jnp.zeros((pad + (8 if d == 0 else 0), rows_dev), jnp.float32)
        return jnp.concatenate([g, q_band[d][None, :], rows], axis=0)

    student_f = student.astype(jnp.float32)
    row_total = jnp.zeros((rows_dev,), jnp.float32)
    pulled = jnp.zeros(student.shape, jnp.float32)
    pulled_band = jnp.zeros(student.shape, jnp.float32)
    own_q = None
    split = min(3, len(offsets))
    for group_idx in ([[0], list(range(split, len(offsets))), list(range(1, split))]):
        if not group_idx:
            continue
        total = width_sum(jnp.stack([tile_part(d) for d in group_idx]))
        if own_q is None:
            own_q = total[0, rows_dev, :]
        for k, d in enumerate(group_idx):
            e = offsets[d]
            resid = own_q[:, None] + total[k, rows_dev, :][None, :] - total[k, :rows_dev, :]
            if d > 0:
                valid = jnp.logical_and(owner + e >= 0, owner + e < group)
                resid = jnp.where(valid, resid, jnp.zeros_like(resid))
            low = resid.astype(jnp.bfloat16)
            row_total = row_total + jnp.sum(resid, axis=1)
            if d == 0:
                pulled = pulled + jnp.dot(low, student_band[d], preferred_element_type=jnp.float32)
            else:
                pulled_band = pulled_band + jnp.dot(low, student_band[d], preferred_element_type=jnp.float32)
            if d > 0:
                back = lax.dot_general(low, student, (((0,), (0,)), ((), ())), preferred_element_type=jnp.float32)
                col = jnp.sum(resid, axis=0)
                if fs == rows_dev:
                    got = shifted(jnp.concatenate([back, col[None, :]], axis=0), "batch", -e)
                    pulled = pulled + got[:rows_dev]
                    row_total = row_total + got[rows_dev]
                else:
                    back_r, col_r = shifted((back, col), "batch", -e)
                    pulled = pulled + back_r
                    row_total = row_total + col_r
    pulled = pulled + pulled_band * (ds / 2.0)
    grad = (student_f * row_total[:, None] - pulled) / near_count
    return grad


def solution(mesh):
    in_specs = (P("batch", "width"), P("batch", "width"))
    out_specs = P("batch", "width")
    return jax.shard_map(layer, mesh=mesh, in_specs=in_specs, out_specs=out_specs, check_vma=False)
```
